256 devices in a mesh: seq: 16 (over z_lo, y), grp: 16 (over x, z_hi, core).
Axes of the slice: x: 4, y: 4, z: 8 (z_hi: 2, z_lo: 4; z = z_hi * 4 + z_lo), core: 2. Of those that a mesh axis runs over, the one named last changes fastest.
Arguments:
- pre_x: bfloat16 [8192, 16384], P('seq', 'grp'), may hold values from -6 to 6
- pre_b: bfloat16 [8192, 2048], P('seq'), may hold values from -6 to 6
- pre_c: bfloat16 [8192, 2048], P('seq'), may hold values from -6 to 6
- pre_dt: float32 [256, 8192], P('grp', 'seq'), may hold values from 0.004 to 0.016
- decay_rate: float32 [256], replicated, may hold values from 0.00390625 to 5
- skip_gain: float32 [256], replicated, may hold values from 0.5 to 1.5
- conv_taps: float32 [4, 20480], replicated, may hold values from -3 to 3
- dec_x: bfloat16 [2, 128, 16384], P(None, 'grp', 'seq'), may hold values from -6 to 6
- dec_b: bfloat16 [2, 128, 2048], P(None, 'grp'), may hold values from -6 to 6
- dec_c: bfloat16 [2, 128, 2048], P(None, 'grp'), may hold values from -6 to 6
- dec_dt: float32 [2, 128, 256], P(None, 'grp', 'seq'), may hold values from 0.004 to 0.016
- dec_query: bfloat16 [2, 128, 8192], P(None, 'grp'), may hold values from -12 to 12
- new_kv: bfloat16 [2, 2, 128, 1024], P(None, None, 'grp'), may hold values from -6 to 6
- cache_kv: bfloat16 [2, 128, 1024, 1024], P(None, 'grp', 'seq'), may hold values from -12 to 12
- kv_len: int32 [128], P('grp'), may hold values from 2 to 1024, as said below
Outputs:
- pre_y: bfloat16 [8192, 16384], P('seq', 'grp')
- dec_y: bfloat16 [2, 128, 16384], P(None, 'grp', 'seq')
- attn_out: bfloat16 [2, 128, 8192], P(None, 'grp', 'seq')
The draws below stay inside these ranges and needn't reach their ends.
Inputs may be any that keep to these rules, and one draw needn't show every extreme that they name: `kv_len`: row 0 of every group of 8 rows has all 1024 positions valid.
All inputs are finite; a program needn't handle non-finite values.
Results may differ from the reference program's by a relative error of at most 0.0013.
Values sent between devices are 32-bit elements; how exact they have to be, the bound alone decides.
No kernel may reach another device: no remote copies, remote signals or barrier semaphores. Data moves between devices by JAX's collectives and lax.ppermute only.
A program may use at most 128 MiB of HBM per device.

```python
import math
import jax
import jax.numpy as jnp
from jax import lax

HEADS = 256
HDIM = 64
STATE = 256
GROUPS = 8
TAPS = 4
QHEADS = 64
KVHEADS = 8
ADIM = 128
SPAN = 256
STEPS = 2
ROWS_GRP = 8
PROMPT = 8192
ROWS = 128
CACHE = 1024


def draw_dec_query(key, part):
    drawn = jax.random.truncated_normal(jax.random.fold_in(key, 11), -6.0, 6.0, (STEPS, ROWS, QHEADS * ADIM), jnp.float32)
    return drawn.astype(jnp.bfloat16)


def draw_cache_kv(key, part):
    drawn = jax.random.truncated_normal(jax.random.fold_in(key, 12), -6.0, 6.0, (2, ROWS, CACHE, KVHEADS * ADIM), jnp.float32)
    return drawn.astype(jnp.bfloat16)


def draw_kv_len(key, part):
    lengths = jax.random.randint(jax.random.fold_in(key, 13), (ROWS,), 2, CACHE + 1)
    row_ids = jnp.arange(ROWS)
    return jnp.where(row_ids % ROWS_GRP == 0, CACHE, lengths).astype(jnp.int32)


def steps_of(key, extent, pieces, smallest, top_value):
    def one(axis_at, shards_of):
        draws = jax.random.uniform(jax.random.fold_in(jax.random.fold_in(key, 6), axis_at), (shards_of,), jnp.float32, smallest / len(pieces), top_value / len(pieces))
        return jnp.repeat(jnp.exp(draws), extent[axis_at] // shards_of).reshape((-1,) + (1,) * (len(extent) - axis_at - 1))

    level = one(*pieces[0])
    for cut in pieces[1:]:
        level = level * one(*cut)
    return level


def scatter_about(key, extent, deviation, limit, shards=(), kind=jnp.bfloat16):
    gain = steps_of(key, extent, shards, -0.22, 0.18) if shards else 1.0
    values = jax.random.normal(key, extent, jnp.float32) * deviation * gain
    return jnp.minimum(jnp.maximum(values, -limit), limit).astype(kind)


def setup_inputs(seed: int = 0) -> dict:
    key_list = jax.random.split(jax.random.key(seed), 16)
    return {
        "pre_x": scatter_about(key_list[0], (PROMPT, HEADS * HDIM), 1.0, 6.0, ((0, 16), (1, 16))),
        "pre_b": scatter_about(key_list[1], (PROMPT, GROUPS * STATE), 1.0, 6.0, ((0, 16),)),
        "pre_c": scatter_about(key_list[2], (PROMPT, GROUPS * STATE), 1.0, 6.0, ((0, 16),)),
        "pre_dt": jnp.clip(jnp.exp(math.log(0.016) - 1.3862944 * jax.random.uniform(key_list[3], (HEADS, PROMPT), jnp.float32) ** steps_of(key_list[3], (HEADS, PROMPT), ((0, 16), (1, 16)), -0.2, 0.2)), 0.004, 0.016),
        "decay_rate": jnp.clip(jnp.exp(jax.random.uniform(key_list[4], (HEADS,), jnp.float32, math.log(0.00390625), math.log(5.0))), 0.00390625, 5.0),
        "skip_gain": jnp.clip(1.0 + 0.1 * jax.random.normal(key_list[5], (HEADS,), jnp.float32), 0.5, 1.5),
        "conv_taps": scatter_about(key_list[6], (TAPS, HEADS * HDIM + 2 * GROUPS * STATE), 0.5, 3.0, (), jnp.float32),
        "dec_x": scatter_about(key_list[7], (STEPS, ROWS, HEADS * HDIM), 1.0, 6.0, ((1, 16), (2, 16))),
        "dec_b": scatter_about(key_list[8], (STEPS, ROWS, GROUPS * STATE), 1.0, 6.0, ((1, 16),)),
        "dec_c": scatter_about(key_list[9], (STEPS, ROWS, GROUPS * STATE), 1.0, 6.0, ((1, 16),)),
        "dec_dt": jnp.clip(jnp.exp(math.log(0.016) - 1.3862944 * jax.random.uniform(key_list[10], (STEPS, ROWS, HEADS), jnp.float32) ** steps_of(key_list[10], (STEPS, ROWS, HEADS), ((1, 16), (2, 16)), -0.2, 0.2)), 0.004, 0.016),
        "dec_query": draw_dec_query(jax.random.fold_in(key_list[15], 71), 0),
        "new_kv": scatter_about(key_list[12], (2, STEPS, ROWS, KVHEADS * ADIM), 1.0, 6.0, ((2, 16),)),
        "cache_kv": draw_cache_kv(jax.random.fold_in(key_list[15], 71), 0),
        "kv_len": draw_kv_len(jax.random.fold_in(key_list[15], 71), 0),
    }


HIGH = lax.Precision.HIGHEST
NEG = -1.0e30


def causal_conv(leading, source, kernel):
    row_total = source.shape[0]
    padded = jnp.concatenate([leading, source], axis=0)
    accumulated = jnp.zeros_like(source)
    for position in range(TAPS):
        accumulated = accumulated + kernel[position] * padded[position:position + row_total]
    return jax.nn.silu(accumulated)


def decode_conv(leading, fresh, kernel):
    results = []
    for current in range(fresh.shape[0]):
        accumulated = jnp.zeros(fresh.shape[1:], jnp.float32)
        for position in range(TAPS):
            place = current + position
            if place < TAPS - 1:
                term = leading[place][None, :]
            else:
                term = fresh[place - (TAPS - 1)]
            accumulated = accumulated + kernel[position] * term
        results.append(jax.nn.silu(accumulated))
    return jnp.stack(results)


def span_pass(ssm_state, block):
    inputs, entries, readout, log_decay = block
    cumulative = jnp.cumsum(log_decay, axis=1)
    block_size = log_decay.shape[1]
    causal = jnp.arange(block_size)[:, None] >= jnp.arange(block_size)[None, :]
    spreads = cumulative[:, :, None] - cumulative[:, None, :]
    weights = jnp.where(causal[None], jnp.exp(jnp.where(causal[None], spreads, 0.0)), 0.0)
    intersection = jnp.dot(readout, entries.T, precision=HIGH)
    intra_span = jnp.einsum('kts,skp->tkp', weights * intersection[None], inputs, precision=HIGH)
    carried = jnp.exp(cumulative).T[:, :, None] * jnp.einsum('tn,kpn->tkp', readout, ssm_state, precision=HIGH)
    remaining = jnp.exp(cumulative[:, -1:] - cumulative)
    updates = jnp.einsum('skp,sn->kpn', inputs * remaining.T[:, :, None], entries, precision=HIGH)
    renewed = jnp.exp(cumulative[:, -1])[:, None, None] * ssm_state + updates
    return renewed, intra_span + carried


def run_spans(inputs, entries, readout, log_decay, ssm_state):
    row_total, heads_here, head_width = inputs.shape
    block_total = row_total // SPAN
    blocks = (inputs.reshape(block_total, SPAN, heads_here, head_width),
              entries.reshape(block_total, SPAN, entries.shape[1]),
              readout.reshape(block_total, SPAN, readout.shape[1]),
              log_decay.reshape(heads_here, block_total, SPAN).transpose(1, 0, 2))
    ssm_state, results = lax.scan(span_pass, ssm_state, blocks)
    return results.reshape(row_total, heads_here, head_width), ssm_state


def decode_mamba(ssm_state, heads_x, heads_b, heads_c, step_dt, rates, gains):
    decays = jnp.exp(-step_dt * rates)
    from_prefix = jnp.einsum('jrhn,hpn->jrhp', heads_c, ssm_state, precision=HIGH)
    results = []
    for current in range(heads_x.shape[0]):
        factor = jnp.ones(decays.shape[1:], jnp.float32)
        accumulated = gains[None, :, None] * heads_x[current]
        for earlier in range(current, -1, -1):
            intersection = jnp.sum(heads_c[current] * heads_b[earlier], axis=-1)
            accumulated = accumulated + (factor * step_dt[earlier] * intersection)[..., None] * heads_x[earlier]
            factor = factor * decays[earlier]
        accumulated = accumulated + factor[..., None] * from_prefix[current]
        results.append(accumulated)
    return jnp.stack(results)


def reference(pre_x, pre_b, pre_c, pre_dt, decay_rate, skip_gain, conv_taps, dec_x, dec_b, dec_c, dec_dt, dec_query, new_kv, cache_kv, kv_len):
    per_group = HEADS // GROUPS
    edge = TAPS - 1
    x_offset = HEADS * HDIM
    c_offset = HEADS * HDIM + GROUPS * STATE

    def one_group(group_id):
        source_x = lax.dynamic_slice_in_dim(pre_x, group_id * per_group * HDIM, per_group * HDIM, 1).astype(jnp.float32)
        source_b = lax.dynamic_slice_in_dim(pre_b, group_id * STATE, STATE, 1).astype(jnp.float32)
        source_c = lax.dynamic_slice_in_dim(pre_c, group_id * STATE, STATE, 1).astype(jnp.float32)
        kernel_x = lax.dynamic_slice_in_dim(conv_taps, group_id * per_group * HDIM, per_group * HDIM, 1)
        kernel_b = lax.dynamic_slice_in_dim(conv_taps, x_offset + group_id * STATE, STATE, 1)
        kernel_c = lax.dynamic_slice_in_dim(conv_taps, c_offset + group_id * STATE, STATE, 1)
        conv_x = causal_conv(jnp.zeros((edge, per_group * HDIM), jnp.float32), source_x, kernel_x)
        conv_b = causal_conv(jnp.zeros((edge, STATE), jnp.float32), source_b, kernel_b)
        conv_c = causal_conv(jnp.zeros((edge, STATE), jnp.float32), source_c, kernel_c)
        step_sizes = lax.dynamic_slice_in_dim(pre_dt, group_id * per_group, per_group, 0)
        rates = lax.dynamic_slice_in_dim(decay_rate, group_id * per_group, per_group, 0)
        gains = lax.dynamic_slice_in_dim(skip_gain, group_id * per_group, per_group, 0)
        log_decay = -step_sizes * rates[:, None]
        head_inputs = conv_x.reshape(PROMPT, per_group, HDIM)
        scaled = head_inputs * step_sizes.T[:, :, None]
        blank = jnp.zeros((per_group, HDIM, STATE), jnp.float32)
        results, closing = run_spans(scaled, conv_b, conv_c, log_decay, blank)
        outputs = results + gains[None, :, None] * head_inputs
        return outputs.reshape(PROMPT, per_group * HDIM).astype(jnp.bfloat16), closing

    group_ids = jnp.arange(GROUPS, dtype=jnp.int32)
    stacked_y, closings = lax.map(one_group, group_ids)
    pre_y = stacked_y.transpose(1, 0, 2).reshape(PROMPT, HEADS * HDIM)
    prefix_state = closings.reshape(HEADS, HDIM, STATE)

    tail_x = pre_x[PROMPT - edge:].astype(jnp.float32)
    tail_b = pre_b[PROMPT - edge:].astype(jnp.float32)
    tail_c = pre_c[PROMPT - edge:].astype(jnp.float32)
    step_x = decode_conv(tail_x, dec_x.astype(jnp.float32), conv_taps[:, :x_offset])
    step_b = decode_conv(tail_b, dec_b.astype(jnp.float32), conv_taps[:, x_offset:c_offset])
    step_c = decode_conv(tail_c, dec_c.astype(jnp.float32), conv_taps[:, c_offset:])
    heads_x = step_x.reshape(STEPS, ROWS, HEADS, HDIM)
    heads_b = jnp.repeat(step_b.reshape(STEPS, ROWS, GROUPS, STATE), per_group, axis=2)
    heads_c = jnp.repeat(step_c.reshape(STEPS, ROWS, GROUPS, STATE), per_group, axis=2)
    mamba_out = decode_mamba(prefix_state, heads_x, heads_b, heads_c, dec_dt, decay_rate, skip_gain)
    dec_y = mamba_out.reshape(STEPS, ROWS, HEADS * HDIM).astype(jnp.bfloat16)

    group_size = QHEADS // KVHEADS
    score_scale = ADIM ** -0.5

    def attend_row(packed):
        query_row, cached_keys, cached_values, fresh_keys, fresh_values, valid_length = packed
        queries = query_row.astype(jnp.float32).reshape(STEPS, KVHEADS, group_size, ADIM)
        key_rows = cached_keys.astype(jnp.float32).reshape(CACHE, KVHEADS, ADIM)
        value_rows = cached_values.astype(jnp.float32).reshape(CACHE, KVHEADS, ADIM)
        new_keys = fresh_keys.astype(jnp.float32).reshape(STEPS, KVHEADS, ADIM)
        new_values = fresh_values.astype(jnp.float32).reshape(STEPS, KVHEADS, ADIM)
        cache_scores = jnp.einsum('jkgd,ckd->jkgc', queries, key_rows, precision=HIGH) * score_scale
        usable = (jnp.arange(CACHE) < valid_length)[None, None, None, :]
        cache_scores = jnp.where(usable, cache_scores, NEG)
        new_scores = jnp.einsum('jkgd,ikd->jkgi', queries, new_keys, precision=HIGH) * score_scale
        allowed = (jnp.arange(STEPS)[None, :] <= jnp.arange(STEPS)[:, None])[:, None, None, :]
        new_scores = jnp.where(allowed, new_scores, NEG)
        peak_score = jnp.maximum(jnp.max(cache_scores, axis=-1), jnp.max(new_scores, axis=-1))
        cache_weights = jnp.where(usable, jnp.exp(cache_scores - peak_score[..., None]), 0.0)
        new_weights = jnp.where(allowed, jnp.exp(new_scores - peak_score[..., None]), 0.0)
        weight_sum = jnp.sum(cache_weights, axis=-1) + jnp.sum(new_weights, axis=-1)
        summed = jnp.einsum('jkgc,ckd->jkgd', cache_weights, value_rows, precision=HIGH)
        summed = summed + jnp.einsum('jkgi,ikd->jkgd', new_weights, new_values, precision=HIGH)
        return (summed / weight_sum[..., None]).reshape(STEPS, QHEADS * ADIM)

    packed_rows = (dec_query.transpose(1, 0, 2), cache_kv[0], cache_kv[1],
                   new_kv[0].transpose(1, 0, 2), new_kv[1].transpose(1, 0, 2), kv_len)
    attended = lax.map(attend_row, packed_rows)
    attn_out = attended.transpose(1, 0, 2).astype(jnp.bfloat16)
    return pre_y, dec_y, attn_out
```

```python
import jax
import jax.numpy as jnp
from jax import lax
from jax.sharding import PartitionSpec as P

HEADS = 256
HDIM = 64
STATE = 256
GROUPS = 8
TAPS = 4
QHEADS = 64
KVHEADS = 8
ADIM = 128
SPAN = 256
STEPS = 2


HIGH = lax.Precision.HIGHEST
NEG = -1e30


def passed_along(value, axis, steps):
    count = lax.axis_size(axis)
    first, last = (max(0, -steps), min(count, count - steps))
    return lax.ppermute(value, axis, [(source, source + steps) for source in range(first, last)])


def causal_conv(leading, source, kernel):
    row_total = source.shape[0]
    padded = jnp.concatenate([leading, source], axis=0)
    accumulated = jnp.zeros_like(source)
    for position in range(TAPS):
        accumulated = accumulated + kernel[position] * padded[position : position + row_total]
    return jax.nn.silu(accumulated)


def decode_conv(leading, fresh, kernel):
    results = []
    for current in range(fresh.shape[0]):
        accumulated = jnp.zeros(fresh.shape[1:], jnp.float32)
        for position in range(TAPS):
            place = current + position
            if place < TAPS - 1:
                term = leading[place][None, :]
            else:
                term = fresh[place - (TAPS - 1)]
            accumulated = accumulated + kernel[position] * term
        results.append(jax.nn.silu(accumulated))
    return jnp.stack(results)


def span_pass(ssm_state, block):
    inputs, entries, readout, log_decay = block
    cumulative = jnp.cumsum(log_decay, axis=1)
    block_size = log_decay.shape[1]
    causal = jnp.arange(block_size)[:, None] >= jnp.arange(block_size)[None, :]
    spreads = cumulative[:, :, None] - cumulative[:, None, :]
    weights = jnp.where(causal[None], jnp.exp(jnp.where(causal[None], spreads, 0.0)), 0.0)
    intersection = jnp.dot(readout, entries.T, precision=HIGH)
    intra_span = jnp.einsum("kts,skp->tkp", weights * intersection[None], inputs, precision=HIGH)
    carried = jnp.exp(cumulative).T[:, :, None] * jnp.einsum(
        "tn,kpn->tkp", readout, ssm_state, precision=HIGH
    )
    remaining = jnp.exp(cumulative[:, -1:] - cumulative)
    updates = jnp.einsum("skp,sn->kpn", inputs * remaining.T[:, :, None], entries, precision=HIGH)
    renewed = jnp.exp(cumulative[:, -1])[:, None, None] * ssm_state + updates
    return (renewed, intra_span + carried)


def decode_mamba(ssm_state, heads_x, heads_b, heads_c, step_dt, rates, gains):
    decays = jnp.exp(-step_dt * rates)
    from_prefix = jnp.einsum("jrhn,hpn->jrhp", heads_c, ssm_state, precision=HIGH)
    results = []
    for current in range(heads_x.shape[0]):
        factor = jnp.ones(decays.shape[1:], jnp.float32)
        accumulated = gains[None, :, None] * heads_x[current]
        for earlier in range(current, -1, -1):
            intersection = jnp.sum(heads_c[current] * heads_b[earlier], axis=-1)
            accumulated = (
                accumulated
                + (factor * step_dt[earlier] * intersection)[..., None] * heads_x[earlier]
            )
            factor = factor * decays[earlier]
        accumulated = accumulated + factor[..., None] * from_prefix[current]
        results.append(accumulated)
    return jnp.stack(results)


def run_spans(inputs, entries, readout, log_decay, ssm_state):
    row_total, heads_here, head_width = inputs.shape
    block_total = row_total // SPAN
    results = []
    for block in range(block_total):
        rows = slice(block * SPAN, (block + 1) * SPAN)
        ssm_state, result = span_pass(
            ssm_state, (inputs[rows], entries[rows], readout[rows], log_decay[:, rows])
        )
        results.append(result)
    return (jnp.concatenate(results, axis=0), ssm_state)


def group_layout(head_begin, head_count):
    per_group = HEADS // GROUPS
    group_count = max(1, head_count // per_group)
    return (head_begin // per_group, group_count, head_count // group_count)


def on_device(
    pre_x,
    pre_b,
    pre_c,
    pre_dt,
    decay_rate,
    skip_gain,
    conv_taps,
    dec_x,
    dec_b,
    dec_c,
    dec_dt,
    dec_query,
    new_kv,
    cache_kv,
    kv_len,
):
    seq_count = lax.axis_size("seq")
    grp_count = lax.axis_size("grp")
    seq_index = lax.axis_index("seq")
    grp_index = lax.axis_index("grp")
    section = pre_x.shape[0]
    local_heads = pre_x.shape[1] // HDIM
    edge = TAPS - 1
    x_offset = HEADS * HDIM
    c_offset = HEADS * HDIM + GROUPS * STATE
    head_begin = grp_index * local_heads
    group_begin, group_count, heads_each = group_layout(head_begin, local_heads)
    source_x = pre_x.astype(jnp.float32)
    group_b = lax.dynamic_slice_in_dim(pre_b, group_begin * STATE, group_count * STATE, 1).astype(
        jnp.float32
    )
    group_c = lax.dynamic_slice_in_dim(pre_c, group_begin * STATE, group_count * STATE, 1).astype(
        jnp.float32
    )
    tail_rows = (source_x[section - edge :], group_b[section - edge :], group_c[section - edge :])
    leading = passed_along(tail_rows, "seq", 1)
    kernel_x = lax.dynamic_slice_in_dim(conv_taps, head_begin * HDIM, local_heads * HDIM, 1)
    kernel_b = lax.dynamic_slice_in_dim(
        conv_taps, x_offset + group_begin * STATE, group_count * STATE, 1
    )
    kernel_c = lax.dynamic_slice_in_dim(
        conv_taps, c_offset + group_begin * STATE, group_count * STATE, 1
    )
    conv_x = causal_conv(leading[0], source_x, kernel_x)
    conv_b = causal_conv(leading[1], group_b, kernel_b)
    conv_c = causal_conv(leading[2], group_c, kernel_c)
    rates = lax.dynamic_slice_in_dim(decay_rate, head_begin, local_heads, 0)
    gains = lax.dynamic_slice_in_dim(skip_gain, head_begin, local_heads, 0)
    log_decay = -pre_dt * rates[:, None]
    head_inputs = conv_x.reshape(section, local_heads, HDIM)
    scaled = head_inputs * pre_dt.T[:, :, None]
    grouped = scaled.reshape(section, group_count, heads_each, HDIM).transpose(1, 0, 2, 3)
    entries = conv_b.reshape(section, group_count, STATE).transpose(1, 0, 2)
    readout = conv_c.reshape(section, group_count, STATE).transpose(1, 0, 2)
    decay_groups = log_decay.reshape(group_count, heads_each, section)
    blank = jnp.zeros((group_count, heads_each, HDIM, STATE), jnp.float32)
    intra_part, closing_local = jax.vmap(run_spans)(grouped, entries, readout, decay_groups, blank)
    local_state = closing_local.reshape(local_heads, HDIM, STATE)
    cumulative = jnp.cumsum(log_decay, axis=1)
    section_decay = cumulative[:, -1]

    rows_here = dec_x.shape[1]
    group_size = QHEADS // KVHEADS
    score_scale = ADIM ** (-0.5)
    positions = cache_kv.shape[2]
    queries = dec_query.reshape(STEPS, rows_here, KVHEADS, group_size, ADIM)
    key_rows = cache_kv[0].reshape(rows_here, positions, KVHEADS, ADIM)
    value_rows = cache_kv[1].reshape(rows_here, positions, KVHEADS, ADIM).astype(jnp.float32)
    scores = (
        jnp.einsum("jrkgd,rckd->jrkgc", queries, key_rows, preferred_element_type=jnp.float32)
        * score_scale
    )
    places = seq_index * positions + jnp.arange(positions)
    usable = (places[None, :] < kv_len[:, None])[None, :, None, None, :]
    scores = jnp.where(usable, scores, NEG)
    peak_local = jnp.max(scores, axis=-1)
    weights = jnp.where(usable, jnp.exp(scores - peak_local[..., None]), 0.0)
    mass_local = jnp.sum(weights, axis=-1)
    summed_local = jnp.einsum("jrkgc,rckd->jrkgd", weights, value_rows, precision=HIGH)
    own_heads = QHEADS // seq_count

    def by_owner(part):
        shaped = part.reshape((STEPS, rows_here, seq_count, own_heads) + part.shape[4:])
        moved = jnp.moveaxis(shaped, 2, 0)
        return moved.reshape(seq_count, -1)

    chunk_heads = local_heads // seq_count
    tail_x_parts = (
        tail_rows[0].reshape(edge, seq_count, chunk_heads * HDIM).transpose(1, 0, 2).reshape(seq_count, -1)
    )
    tail_bc = jnp.concatenate([tail_rows[1], tail_rows[2]], axis=0).reshape(seq_count, -1)
    pieces = [
        local_state.reshape(seq_count, -1),
        section_decay.reshape(seq_count, chunk_heads),
        tail_x_parts,
        tail_bc,
    ]
    sizes = [piece.shape[1] for piece in pieces]
    attn_pieces = [by_owner(peak_local), by_owner(mass_local), by_owner(summed_local)]
    attn_sizes = [piece.shape[1] for piece in attn_pieces]
    payload = jnp.concatenate(pieces + attn_pieces, axis=1)
    width = payload.shape[1]
    padded = -(-width // 128) * 128
    payload = jnp.pad(payload, ((0, 0), (0, padded - width)))
    arrived = lax.all_to_all(payload, "seq", 0, 0, tiled=True)
    bounds = [0]
    for size in sizes + attn_sizes:
        bounds.append(bounds[-1] + size)
    got = [arrived[:, bounds[i] : bounds[i + 1]] for i in range(len(bounds) - 1)]
    states_in, decays_in, tail_x_in, tail_bc_in, peak_in, mass_in, summed_in = got

    carry = jnp.zeros((chunk_heads, HDIM * STATE), jnp.float32)
    entering = []
    states_in = states_in.reshape(seq_count, chunk_heads, HDIM * STATE)
    for source in range(seq_count):
        entering.append(carry)
        carry = jnp.exp(decays_in[source])[:, None] * carry + states_in[source]
    entering = jnp.stack(entering).reshape(seq_count, -1)
    returned = lax.all_to_all(entering, "seq", 0, 0, tiled=True)
    incoming = returned.reshape(local_heads, HDIM, STATE)

    handoff = jnp.concatenate(
        [carry.reshape(-1), tail_x_in[seq_count - 1], tail_bc_in[seq_count - 1]], axis=0
    )
    swap = [
        (a * grp_count + b, b * grp_count + a) for a in range(seq_count) for b in range(grp_count)
    ]
    swapped = lax.ppermute(handoff, ("seq", "grp"), swap)
    gathered = lax.all_gather(swapped, "grp")
    state_size = chunk_heads * HDIM * STATE
    tail_size = tail_x_in.shape[1]
    state_heads = HEADS // seq_count
    prefix_state = gathered[:, :state_size].reshape(state_heads, HDIM, STATE)
    prefix_tail = (
        gathered[:, state_size : state_size + tail_size]
        .reshape(grp_count, edge, chunk_heads * HDIM)
        .transpose(1, 0, 2)
        .reshape(edge, state_heads * HDIM)
    )
    dgroup_width = tail_rows[1].shape[1]
    tail_bc_all = gathered[:, state_size + tail_size :].reshape(2 * edge, dgroup_width)
    tail_b = tail_bc_all[:edge]
    tail_c = tail_bc_all[edge:]

    incoming_groups = incoming.reshape(group_count, heads_each, HDIM, STATE)
    from_before = jnp.einsum("gsn,gkpn->gskp", readout, incoming_groups, precision=HIGH)
    decay_factor = jnp.exp(cumulative).reshape(group_count, heads_each, section).transpose(0, 2, 1)
    combined = intra_part + decay_factor[..., None] * from_before
    combined = (
        combined.transpose(1, 0, 2, 3).reshape(section, local_heads, HDIM)
        + gains[None, :, None] * head_inputs
    )
    pre_y = combined.reshape(section, local_heads * HDIM).astype(jnp.bfloat16)

    dec_begin = seq_index * state_heads
    dgroup_begin, dgroup_count, dheads_each = group_layout(dec_begin, state_heads)
    kernel_dx = lax.dynamic_slice_in_dim(conv_taps, dec_begin * HDIM, state_heads * HDIM, 1)
    kernel_db = lax.dynamic_slice_in_dim(
        conv_taps, x_offset + dgroup_begin * STATE, dgroup_count * STATE, 1
    )
    kernel_dc = lax.dynamic_slice_in_dim(
        conv_taps, c_offset + dgroup_begin * STATE, dgroup_count * STATE, 1
    )
    step_x = decode_conv(prefix_tail, dec_x.astype(jnp.float32), kernel_dx)
    step_b = decode_conv(
        tail_b,
        lax.dynamic_slice_in_dim(dec_b, dgroup_begin * STATE, dgroup_count * STATE, 2).astype(
            jnp.float32
        ),
        kernel_db,
    )
    step_c = decode_conv(
        tail_c,
        lax.dynamic_slice_in_dim(dec_c, dgroup_begin * STATE, dgroup_count * STATE, 2).astype(
            jnp.float32
        ),
        kernel_dc,
    )
    heads_x = step_x.reshape(STEPS, rows_here, state_heads, HDIM)
    heads_b = jnp.repeat(step_b.reshape(STEPS, rows_here, dgroup_count, STATE), dheads_each, axis=2)
    heads_c = jnp.repeat(step_c.reshape(STEPS, rows_here, dgroup_count, STATE), dheads_each, axis=2)
    dec_rates = lax.dynamic_slice_in_dim(decay_rate, dec_begin, state_heads, 0)
    dec_gains = lax.dynamic_slice_in_dim(skip_gain, dec_begin, state_heads, 0)
    mamba_out = decode_mamba(prefix_state, heads_x, heads_b, heads_c, dec_dt, dec_rates, dec_gains)
    dec_y = mamba_out.reshape(STEPS, rows_here, state_heads * HDIM).astype(jnp.bfloat16)

    peak_in = peak_in.reshape(seq_count, STEPS, rows_here, own_heads)
    mass_in = mass_in.reshape(seq_count, STEPS, rows_here, own_heads)
    summed_in = summed_in.reshape(seq_count, STEPS, rows_here, own_heads, ADIM)
    peak_cache = jnp.max(peak_in, axis=0)
    part_scale = jnp.exp(peak_in - peak_cache[None])
    mass_cache = jnp.sum(mass_in * part_scale, axis=0)
    summed_cache = jnp.sum(summed_in * part_scale[..., None], axis=0)
    head_start = seq_index * own_heads
    new_keys = new_kv[0].reshape(STEPS, rows_here, KVHEADS, ADIM)
    new_values = new_kv[1].reshape(STEPS, rows_here, KVHEADS, ADIM).astype(jnp.float32)
    new_scores = (
        jnp.einsum("jrkgd,irkd->jrkgi", queries, new_keys, preferred_element_type=jnp.float32)
        * score_scale
    )
    allowed = (jnp.arange(STEPS)[None, :] <= jnp.arange(STEPS)[:, None])[:, None, None, None, :]
    new_scores = jnp.where(allowed, new_scores, NEG)
    new_scores = lax.dynamic_slice_in_dim(
        new_scores.reshape(STEPS, rows_here, QHEADS, STEPS), head_start, own_heads, 2
    )
    allowed_heads = (jnp.arange(STEPS)[None, :] <= jnp.arange(STEPS)[:, None])[:, None, None, :]
    head_kv = (head_start + jnp.arange(own_heads)) // group_size
    pick = (head_kv[:, None] == jnp.arange(KVHEADS)[None, :]).astype(jnp.float32)
    own_values = jnp.einsum("hk,irkd->irhd", pick, new_values, precision=HIGH)
    peak_total = jnp.maximum(peak_cache, jnp.max(new_scores, axis=-1))
    cache_scale = jnp.exp(peak_cache - peak_total)
    new_weights = jnp.where(allowed_heads, jnp.exp(new_scores - peak_total[..., None]), 0.0)
    mass_total = mass_cache * cache_scale + jnp.sum(new_weights, axis=-1)
    summed_total = summed_cache * cache_scale[..., None] + jnp.einsum(
        "jrhi,irhd->jrhd", new_weights, own_values, precision=HIGH
    )
    attn_out = (
        (summed_total / mass_total[..., None])
        .reshape(STEPS, rows_here, own_heads * ADIM)
        .astype(jnp.bfloat16)
    )
    return (pre_y, dec_y, attn_out)


def solution(mesh):
    in_specs = (
        P("seq", "grp"),
        P("seq", None),
        P("seq", None),
        P("grp", "seq"),
        P(),
        P(),
        P(),
        P(None, "grp", "seq"),
        P(None, "grp", None),
        P(None, "grp", None),
        P(None, "grp", "seq"),
        P(None, "grp", None),
        P(None, None, "grp", None),
        P(None, "grp", "seq", None),
        P("grp"),
    )
    out_specs = (P("seq", "grp"), P(None, "grp", "seq"), P(None, "grp", "seq"))
    return jax.shard_map(
        on_device, mesh=mesh, in_specs=in_specs, out_specs=out_specs, check_vma=False
    )
```

```python
import jax
import jax.numpy as jnp
from jax import lax
from jax.sharding import PartitionSpec as P

HEADS = 256
HDIM = 64
STATE = 256
GROUPS = 8
TAPS = 4
QHEADS = 64
KVHEADS = 8
ADIM = 128
SPAN = 256
STEPS = 2


HIGH = lax.Precision.HIGHEST
NEG = -1e30


LANES = 128


def exchanged(pieces, axis):
    count = pieces[0].shape[0]
    sizes = [piece.shape[1] for piece in pieces]
    rows = [-(-size // LANES) for size in sizes]
    packed = jnp.concatenate(
        [
            jnp.pad(piece, ((0, 0), (0, row * LANES - size))).reshape(count, row, LANES)
            for piece, size, row in zip(pieces, sizes, rows)
        ],
        axis=1,
    )
    arrived = lax.all_to_all(packed, axis, 0, 0, tiled=False)
    results = []
    begin = 0
    for size, row in zip(sizes, rows):
        results.append(arrived[:, begin : begin + row].reshape(count, row * LANES)[:, :size])
        begin += row
    return results


def passed_along(value, axis, steps):
    count = lax.axis_size(axis)
    first, last = (max(0, -steps), min(count, count - steps))
    return lax.ppermute(value, axis, [(source, source + steps) for source in range(first, last)])


def causal_conv(leading, source, kernel):
    row_total = source.shape[0]
    padded = jnp.concatenate([leading, source], axis=0)
    accumulated = jnp.zeros_like(source)
    for position in range(TAPS):
        accumulated = accumulated + kernel[position] * padded[position : position + row_total]
    return jax.nn.silu(accumulated)


def decode_conv(leading, fresh, kernel):
    results = []
    for current in range(fresh.shape[0]):
        accumulated = jnp.zeros(fresh.shape[1:], jnp.float32)
        for position in range(TAPS):
            place = current + position
            if place < TAPS - 1:
                term = leading[place][None, :]
            else:
                term = fresh[place - (TAPS - 1)]
            accumulated = accumulated + kernel[position] * term
        results.append(jax.nn.silu(accumulated))
    return jnp.stack(results)


def span_pass(ssm_state, block):
    inputs, entries, readout, log_decay = block
    cumulative = jnp.cumsum(log_decay, axis=1)
    block_size = log_decay.shape[1]
    causal = jnp.arange(block_size)[:, None] >= jnp.arange(block_size)[None, :]
    spreads = cumulative[:, :, None] - cumulative[:, None, :]
    weights = jnp.where(causal[None], jnp.exp(jnp.where(causal[None], spreads, 0.0)), 0.0)
    intersection = jnp.dot(readout, entries.T, precision=HIGH)
    intra_span = jnp.einsum("kts,skp->tkp", weights * intersection[None], inputs, precision=HIGH)
    carried = jnp.exp(cumulative).T[:, :, None] * jnp.einsum(
        "tn,kpn->tkp", readout, ssm_state, precision=HIGH
    )
    remaining = jnp.exp(cumulative[:, -1:] - cumulative)
    updates = jnp.einsum("skp,sn->kpn", inputs * remaining.T[:, :, None], entries, precision=HIGH)
    renewed = jnp.exp(cumulative[:, -1])[:, None, None] * ssm_state + updates
    return (renewed, intra_span + carried)


def decode_mamba(ssm_state, heads_x, heads_b, heads_c, step_dt, rates, gains):
    decays = jnp.exp(-step_dt * rates)
    from_prefix = jnp.einsum("jrhn,hpn->jrhp", heads_c, ssm_state, precision=HIGH)
    results = []
    for current in range(heads_x.shape[0]):
        factor = jnp.ones(decays.shape[1:], jnp.float32)
        accumulated = gains[None, :, None] * heads_x[current]
        for earlier in range(current, -1, -1):
            intersection = jnp.sum(heads_c[current] * heads_b[earlier], axis=-1)
            accumulated = (
                accumulated
                + (factor * step_dt[earlier] * intersection)[..., None] * heads_x[earlier]
            )
            factor = factor * decays[earlier]
        accumulated = accumulated + factor[..., None] * from_prefix[current]
        results.append(accumulated)
    return jnp.stack(results)


def run_spans(inputs, entries, readout, log_decay, ssm_state):
    row_total, _, _ = inputs.shape
    block_total = row_total // SPAN
    results = []
    for block in range(block_total):
        rows = slice(block * SPAN, (block + 1) * SPAN)
        ssm_state, result = span_pass(
            ssm_state, (inputs[rows], entries[rows], readout[rows], log_decay[:, rows])
        )
        results.append(result)
    return (jnp.concatenate(results, axis=0), ssm_state)


def group_layout(head_begin, head_count):
    per_group = HEADS // GROUPS
    group_count = max(1, head_count // per_group)
    return (head_begin // per_group, group_count, head_count // group_count)


def on_device(
    pre_x,
    pre_b,
    pre_c,
    pre_dt,
    decay_rate,
    skip_gain,
    conv_taps,
    dec_x,
    dec_b,
    dec_c,
    dec_dt,
    dec_query,
    new_kv,
    cache_kv,
    kv_len,
):
    seq_count = lax.axis_size("seq")
    grp_count = lax.axis_size("grp")
    seq_index = lax.axis_index("seq")
    grp_index = lax.axis_index("grp")
    section = pre_x.shape[0]
    local_heads = pre_x.shape[1] // HDIM
    edge = TAPS - 1
    x_offset = HEADS * HDIM
    c_offset = HEADS * HDIM + GROUPS * STATE
    head_begin = grp_index * local_heads
    group_begin, group_count, heads_each = group_layout(head_begin, local_heads)
    source_x = pre_x.astype(jnp.float32)
    group_b = lax.dynamic_slice_in_dim(pre_b, group_begin * STATE, group_count * STATE, 1).astype(
        jnp.float32
    )
    group_c = lax.dynamic_slice_in_dim(pre_c, group_begin * STATE, group_count * STATE, 1).astype(
        jnp.float32
    )
    tail_rows = (source_x[section - edge :], group_b[section - edge :], group_c[section - edge :])
    leading = passed_along(tail_rows, "seq", 1)
    kernel_x = lax.dynamic_slice_in_dim(conv_taps, head_begin * HDIM, local_heads * HDIM, 1)
    kernel_b = lax.dynamic_slice_in_dim(
        conv_taps, x_offset + group_begin * STATE, group_count * STATE, 1
    )
    kernel_c = lax.dynamic_slice_in_dim(
        conv_taps, c_offset + group_begin * STATE, group_count * STATE, 1
    )
    conv_x = causal_conv(leading[0], source_x, kernel_x)
    conv_b = causal_conv(leading[1], group_b, kernel_b)
    conv_c = causal_conv(leading[2], group_c, kernel_c)
    rates = lax.dynamic_slice_in_dim(decay_rate, head_begin, local_heads, 0)
    gains = lax.dynamic_slice_in_dim(skip_gain, head_begin, local_heads, 0)
    log_decay = -pre_dt * rates[:, None]
    head_inputs = conv_x.reshape(section, local_heads, HDIM)
    scaled = head_inputs * pre_dt.T[:, :, None]
    grouped = scaled.reshape(section, group_count, heads_each, HDIM).transpose(1, 0, 2, 3)
    entries = conv_b.reshape(section, group_count, STATE).transpose(1, 0, 2)
    readout = conv_c.reshape(section, group_count, STATE).transpose(1, 0, 2)
    decay_groups = log_decay.reshape(group_count, heads_each, section)
    blank = jnp.zeros((group_count, heads_each, HDIM, STATE), jnp.float32)
    intra_part, closing_local = jax.vmap(run_spans)(grouped, entries, readout, decay_groups, blank)
    local_state = closing_local.reshape(local_heads, HDIM, STATE)
    cumulative = jnp.cumsum(log_decay, axis=1)
    section_decay = cumulative[:, -1]

    rows_here = dec_x.shape[1]
    group_size = QHEADS // KVHEADS
    score_scale = ADIM ** (-0.5)
    positions = cache_kv.shape[2]
    queries = dec_query.reshape(STEPS, rows_here, KVHEADS, group_size, ADIM)
    key_rows = cache_kv[0].reshape(rows_here, positions, KVHEADS, ADIM)
    value_rows = cache_kv[1].reshape(rows_here, positions, KVHEADS, ADIM).astype(jnp.float32)
    scores = (
        jnp.einsum("jrkgd,rckd->jrkgc", queries, key_rows, preferred_element_type=jnp.float32)
        * score_scale
    )
    places = seq_index * positions + jnp.arange(positions)
    usable = (places[None, :] < kv_len[:, None])[None, :, None, None, :]
    scores = jnp.where(usable, scores, NEG)
    peak_local = jnp.max(scores, axis=-1)
    weights = jnp.where(usable, jnp.exp(scores - peak_local[..., None]), 0.0)
    mass_local = jnp.sum(weights, axis=-1)
    summed_local = jnp.einsum("jrkgc,rckd->jrkgd", weights, value_rows, precision=HIGH)
    own_heads = QHEADS // seq_count

    def by_owner(part):
        shaped = part.reshape((STEPS, rows_here, seq_count, own_heads) + part.shape[4:])
        moved = jnp.moveaxis(shaped, 2, 0)
        return moved.reshape(seq_count, -1)

    chunk_heads = local_heads // seq_count
    tail_x_parts = (
        tail_rows[0].reshape(edge, seq_count, chunk_heads * HDIM).transpose(1, 0, 2).reshape(seq_count, -1)
    )
    tail_bc = jnp.concatenate([tail_rows[1], tail_rows[2]], axis=0).reshape(seq_count, -1)
    pieces = [
        local_state.reshape(seq_count, -1),
        section_decay.reshape(seq_count, chunk_heads),
        tail_x_parts,
        tail_bc,
    ]
    peak_in, mass_in, summed_in = exchanged(
        [by_owner(peak_local), by_owner(mass_local), by_owner(summed_local)], "seq"
    )
    states_in, decays_in, tail_x_in, tail_bc_in = exchanged(pieces, "seq")

    states_in = states_in.reshape(seq_count, chunk_heads, LANES, -1)
    decays_in = decays_in[:, :chunk_heads]
    after = jnp.arange(seq_count + 1)[:, None, None]
    source = jnp.arange(seq_count)[None, :, None]
    between = jnp.arange(seq_count)[None, None, :]
    spans = ((source < between) & (between < after)).astype(jnp.float32)
    exponents = jnp.sum(spans[None] * decays_in.T[:, None, None, :], axis=-1)
    carry_weights = jnp.where((source < after)[None, :, :, 0], jnp.exp(exponents), 0.0)
    carried_all = jnp.einsum("has,shrc->ahrc", carry_weights, states_in, precision=HIGH)
    entering = carried_all[:seq_count].reshape(seq_count, -1, LANES)
    carry = carried_all[seq_count]
    returned = lax.all_to_all(entering, "seq", 0, 0, tiled=False)
    incoming = returned.reshape(local_heads, HDIM, STATE)

    state_size = chunk_heads * HDIM * STATE
    tail_size = tail_x_parts.shape[1]
    handoff = jnp.concatenate(
        [carry.reshape(-1), tail_x_in[seq_count - 1], tail_bc_in[seq_count - 1]], axis=0
    )
    handoff = jnp.pad(handoff, (0, -handoff.shape[0] % LANES)).reshape(-1, LANES)
    swap = [
        (a * grp_count + b, b * grp_count + a) for a in range(seq_count) for b in range(grp_count)
    ]
    swapped = lax.ppermute(handoff, ("seq", "grp"), swap)
    copies = jnp.broadcast_to(swapped[None], (grp_count,) + swapped.shape)
    gathered = lax.all_to_all(copies, "grp", 0, 0, tiled=False).reshape(grp_count, -1)
    state_heads = HEADS // seq_count
    prefix_state = gathered[:, :state_size].reshape(state_heads, HDIM, STATE)
    prefix_tail = (
        gathered[:, state_size : state_size + tail_size]
        .reshape(grp_count, edge, chunk_heads * HDIM)
        .transpose(1, 0, 2)
        .reshape(edge, state_heads * HDIM)
    )
    dgroup_width = tail_rows[1].shape[1]
    bc_size = 2 * edge * dgroup_width // grp_count
    tail_bc_all = gathered[:, state_size + tail_size : state_size + tail_size + bc_size].reshape(
        2 * edge, dgroup_width
    )
    tail_b = tail_bc_all[:edge]
    tail_c = tail_bc_all[edge:]

    incoming_groups = incoming.reshape(group_count, heads_each, HDIM, STATE)
    from_before = jnp.einsum("gsn,gkpn->gskp", readout, incoming_groups, precision=HIGH)
    decay_factor = jnp.exp(cumulative).reshape(group_count, heads_each, section).transpose(0, 2, 1)
    combined = intra_part + decay_factor[..., None] * from_before
    combined = (
        combined.transpose(1, 0, 2, 3).reshape(section, local_heads, HDIM)
        + gains[None, :, None] * head_inputs
    )
    pre_y = combined.reshape(section, local_heads * HDIM).astype(jnp.bfloat16)

    dec_begin = seq_index * state_heads
    dgroup_begin, dgroup_count, dheads_each = group_layout(dec_begin, state_heads)
    kernel_dx = lax.dynamic_slice_in_dim(conv_taps, dec_begin * HDIM, state_heads * HDIM, 1)
    kernel_db = lax.dynamic_slice_in_dim(
        conv_taps, x_offset + dgroup_begin * STATE, dgroup_count * STATE, 1
    )
    kernel_dc = lax.dynamic_slice_in_dim(
        conv_taps, c_offset + dgroup_begin * STATE, dgroup_count * STATE, 1
    )
    step_x = decode_conv(prefix_tail, dec_x.astype(jnp.float32), kernel_dx)
    step_b = decode_conv(
        tail_b,
        lax.dynamic_slice_in_dim(dec_b, dgroup_begin * STATE, dgroup_count * STATE, 2).astype(
            jnp.float32
        ),
        kernel_db,
    )
    step_c = decode_conv(
        tail_c,
        lax.dynamic_slice_in_dim(dec_c, dgroup_begin * STATE, dgroup_count * STATE, 2).astype(
            jnp.float32
        ),
        kernel_dc,
    )
    heads_x = step_x.reshape(STEPS, rows_here, state_heads, HDIM)
    heads_b = jnp.repeat(step_b.reshape(STEPS, rows_here, dgroup_count, STATE), dheads_each, axis=2)
    heads_c = jnp.repeat(step_c.reshape(STEPS, rows_here, dgroup_count, STATE), dheads_each, axis=2)
    dec_rates = lax.dynamic_slice_in_dim(decay_rate, dec_begin, state_heads, 0)
    dec_gains = lax.dynamic_slice_in_dim(skip_gain, dec_begin, state_heads, 0)
    mamba_out = decode_mamba(prefix_state, heads_x, heads_b, heads_c, dec_dt, dec_rates, dec_gains)
    dec_y = mamba_out.reshape(STEPS, rows_here, state_heads * HDIM).astype(jnp.bfloat16)

    head_start = seq_index * own_heads
    new_keys = new_kv[0].reshape(STEPS, rows_here, KVHEADS, ADIM)
    new_values = new_kv[1].reshape(STEPS, rows_here, KVHEADS, ADIM).astype(jnp.float32)
    new_scores = (
        jnp.einsum("jrkgd,irkd->jrkgi", queries, new_keys, preferred_element_type=jnp.float32)
        * score_scale
    )
    allowed = (jnp.arange(STEPS)[None, :] <= jnp.arange(STEPS)[:, None])[:, None, None, None, :]
    new_scores = jnp.where(allowed, new_scores, NEG)
    new_scores = lax.dynamic_slice_in_dim(
        new_scores.reshape(STEPS, rows_here, QHEADS, STEPS), head_start, own_heads, 2
    )
    allowed_heads = (jnp.arange(STEPS)[None, :] <= jnp.arange(STEPS)[:, None])[:, None, None, :]
    head_kv = (head_start + jnp.arange(own_heads)) // group_size
    pick = (head_kv[:, None] == jnp.arange(KVHEADS)[None, :]).astype(jnp.float32)
    own_values = jnp.einsum("hk,irkd->irhd", pick, new_values, precision=HIGH)
    peak_in = peak_in.reshape(seq_count, STEPS, rows_here, own_heads)
    mass_in = mass_in.reshape(seq_count, STEPS, rows_here, own_heads)
    summed_in = summed_in.reshape(seq_count, STEPS, rows_here, own_heads, ADIM)
    peak_cache = jnp.max(peak_in, axis=0)
    part_scale = jnp.exp(peak_in - peak_cache[None])
    mass_cache = jnp.sum(mass_in * part_scale, axis=0)
    summed_cache = jnp.sum(summed_in * part_scale[..., None], axis=0)
    peak_total = jnp.maximum(peak_cache, jnp.max(new_scores, axis=-1))
    cache_scale = jnp.exp(peak_cache - peak_total)
    new_weights = jnp.where(allowed_heads, jnp.exp(new_scores - peak_total[..., None]), 0.0)
    mass_total = mass_cache * cache_scale + jnp.sum(new_weights, axis=-1)
    summed_total = summed_cache * cache_scale[..., None] + jnp.einsum(
        "jrhi,irhd->jrhd", new_weights, own_values, precision=HIGH
    )
    attn_out = (
        (summed_total / mass_total[..., None])
        .reshape(STEPS, rows_here, own_heads * ADIM)
        .astype(jnp.bfloat16)
    )
    return (pre_y, dec_y, attn_out)


def solution(mesh):
    in_specs = (
        P("seq", "grp"),
        P("seq", None),
        P("seq", None),
        P("grp", "seq"),
        P(),
        P(),
        P(),
        P(None, "grp", "seq"),
        P(None, "grp", None),
        P(None, "grp", None),
        P(None, "grp", "seq"),
        P(None, "grp", None),
        P(None, None, "grp", None),
        P(None, "grp", "seq", None),
        P("grp"),
    )
    out_specs = (P("seq", "grp"), P(None, "grp", "seq"), P(None, "grp", "seq"))

    return jax.shard_map(on_device, mesh=mesh, in_specs=in_specs, out_specs=out_specs, check_vma=False)
```

```python
import jax
import jax.numpy as jnp
from jax import lax
from jax.sharding import PartitionSpec as P

HEADS = 256
HDIM = 64
STATE = 256
GROUPS = 8
TAPS = 4
QHEADS = 64
KVHEADS = 8
ADIM = 128
SPAN = 256
STEPS = 2


HIGH = lax.Precision.HIGHEST
NEG = -1e30


LANES = 128


def exchanged(pieces, axis):
    count = pieces[0].shape[0]
    sizes = [piece.shape[1] for piece in pieces]
    rows = [-(-size // LANES) for size in sizes]
    packed = jnp.concatenate(
        [
            jnp.pad(piece, ((0, 0), (0, row * LANES - size))).reshape(count, row, LANES)
            for piece, size, row in zip(pieces, sizes, rows)
        ],
        axis=1,
    )
    arrived = lax.all_to_all(packed, axis, 0, 0, tiled=False)
    results = []
    begin = 0
    for size, row in zip(sizes, rows):
        results.append(arrived[:, begin : begin + row].reshape(count, row * LANES)[:, :size])
        begin += row
    return results


def passed_along(value, axis, steps):
    count = lax.axis_size(axis)
    first, last = (max(0, -steps), min(count, count - steps))
    return lax.ppermute(value, axis, [(source, source + steps) for source in range(first, last)])


def causal_conv(leading, source, kernel):
    row_total = source.shape[0]
    padded = jnp.concatenate([leading, source], axis=0)
    accumulated = jnp.zeros_like(source)
    for position in range(TAPS):
        accumulated = accumulated + kernel[position] * padded[position : position + row_total]
    return jax.nn.silu(accumulated)


def decode_conv(leading, fresh, kernel):
    results = []
    for current in range(fresh.shape[0]):
        accumulated = jnp.zeros(fresh.shape[1:], jnp.float32)
        for position in range(TAPS):
            place = current + position
            if place < TAPS - 1:
                term = leading[place][None, :]
            else:
                term = fresh[place - (TAPS - 1)]
            accumulated = accumulated + kernel[position] * term
        results.append(jax.nn.silu(accumulated))
    return jnp.stack(results)


def span_pass(ssm_state, block):
    inputs, entries, readout, log_decay = block
    cumulative = jnp.cumsum(log_decay, axis=1)
    block_size = log_decay.shape[1]
    causal = jnp.arange(block_size)[:, None] >= jnp.arange(block_size)[None, :]
    spreads = cumulative[:, :, None] - cumulative[:, None, :]
    weights = jnp.where(causal[None], jnp.exp(jnp.where(causal[None], spreads, 0.0)), 0.0)
    intersection = jnp.dot(readout, entries.T, precision=HIGH)
    intra_span = jnp.einsum("kts,skp->tkp", weights * intersection[None], inputs, precision=HIGH)
    carried = jnp.exp(cumulative).T[:, :, None] * jnp.einsum(
        "tn,kpn->tkp", readout, ssm_state, precision=HIGH
    )
    remaining = jnp.exp(cumulative[:, -1:] - cumulative)
    updates = jnp.einsum("skp,sn->kpn", inputs * remaining.T[:, :, None], entries, precision=HIGH)
    renewed = jnp.exp(cumulative[:, -1])[:, None, None] * ssm_state + updates
    return (renewed, intra_span + carried)


def decode_mamba(ssm_state, heads_x, heads_b, heads_c, step_dt, rates, gains):
    decays = jnp.exp(-step_dt * rates)
    from_prefix = jnp.einsum("jrhn,hpn->jrhp", heads_c, ssm_state, precision=HIGH)
    results = []
    for current in range(heads_x.shape[0]):
        factor = jnp.ones(decays.shape[1:], jnp.float32)
        accumulated = gains[None, :, None] * heads_x[current]
        for earlier in range(current, -1, -1):
            intersection = jnp.sum(heads_c[current] * heads_b[earlier], axis=-1)
            accumulated = (
                accumulated
                + (factor * step_dt[earlier] * intersection)[..., None] * heads_x[earlier]
            )
            factor = factor * decays[earlier]
        accumulated = accumulated + factor[..., None] * from_prefix[current]
        results.append(accumulated)
    return jnp.stack(results)


def run_spans(inputs, entries, readout, log_decay, ssm_state):
    row_total, _, _ = inputs.shape
    block_total = row_total // SPAN
    results = []
    for block in range(block_total):
        rows = slice(block * SPAN, (block + 1) * SPAN)
        ssm_state, result = span_pass(
            ssm_state, (inputs[rows], entries[rows], readout[rows], log_decay[:, rows])
        )
        results.append(result)
    return (jnp.concatenate(results, axis=0), ssm_state)


def group_layout(head_begin, head_count):
    per_group = HEADS // GROUPS
    group_count = max(1, head_count // per_group)
    return (head_begin // per_group, group_count, head_count // group_count)


def on_device(
    pre_x,
    pre_b,
    pre_c,
    pre_dt,
    decay_rate,
    skip_gain,
    conv_taps,
    dec_x,
    dec_b,
    dec_c,
    dec_dt,
    dec_query,
    new_kv,
    cache_kv,
    kv_len,
):
    seq_count = lax.axis_size("seq")
    grp_count = lax.axis_size("grp")
    seq_index = lax.axis_index("seq")
    grp_index = lax.axis_index("grp")
    section = pre_x.shape[0]
    local_heads = pre_x.shape[1] // HDIM
    edge = TAPS - 1
    x_offset = HEADS * HDIM
    c_offset = HEADS * HDIM + GROUPS * STATE
    head_begin = grp_index * local_heads
    group_begin, group_count, heads_each = group_layout(head_begin, local_heads)
    source_x = pre_x.astype(jnp.float32)
    group_b = lax.dynamic_slice_in_dim(pre_b, group_begin * STATE, group_count * STATE, 1).astype(
        jnp.float32
    )
    group_c = lax.dynamic_slice_in_dim(pre_c, group_begin * STATE, group_count * STATE, 1).astype(
        jnp.float32
    )
    tail_rows = (source_x[section - edge :], group_b[section - edge :], group_c[section - edge :])
    leading = passed_along(tail_rows, "seq", 1)
    kernel_x = lax.dynamic_slice_in_dim(conv_taps, head_begin * HDIM, local_heads * HDIM, 1)
    kernel_b = lax.dynamic_slice_in_dim(
        conv_taps, x_offset + group_begin * STATE, group_count * STATE, 1
    )
    kernel_c = lax.dynamic_slice_in_dim(
        conv_taps, c_offset + group_begin * STATE, group_count * STATE, 1
    )
    conv_x = causal_conv(leading[0], source_x, kernel_x)
    conv_b = causal_conv(leading[1], group_b, kernel_b)
    conv_c = causal_conv(leading[2], group_c, kernel_c)
    rates = lax.dynamic_slice_in_dim(decay_rate, head_begin, local_heads, 0)
    gains = lax.dynamic_slice_in_dim(skip_gain, head_begin, local_heads, 0)
    log_decay = -pre_dt * rates[:, None]
    head_inputs = conv_x.reshape(section, local_heads, HDIM)
    scaled = head_inputs * pre_dt.T[:, :, None]
    grouped = scaled.reshape(section, group_count, heads_each, HDIM).transpose(1, 0, 2, 3)
    entries = conv_b.reshape(section, group_count, STATE).transpose(1, 0, 2)
    readout = conv_c.reshape(section, group_count, STATE).transpose(1, 0, 2)
    decay_groups = log_decay.reshape(group_count, heads_each, section)
    blank = jnp.zeros((group_count, heads_each, HDIM, STATE), jnp.float32)
    intra_part, closing_local = jax.vmap(run_spans)(grouped, entries, readout, decay_groups, blank)
    local_state = closing_local.reshape(local_heads, HDIM, STATE)
    cumulative = jnp.cumsum(log_decay, axis=1)
    section_decay = cumulative[:, -1]

    rows_here = dec_x.shape[1]
    group_size = QHEADS // KVHEADS
    score_scale = ADIM ** (-0.5)
    positions = cache_kv.shape[2]
    queries = dec_query.reshape(STEPS, rows_here, KVHEADS, group_size, ADIM)
    key_rows = cache_kv[0].reshape(rows_here, positions, KVHEADS, ADIM)
    value_rows = cache_kv[1].reshape(rows_here, positions, KVHEADS, ADIM).astype(jnp.float32)
    scores = (
        jnp.einsum("jrkgd,rckd->jrkgc", queries, key_rows, preferred_element_type=jnp.float32)
        * score_scale
    )
    places = seq_index * positions + jnp.arange(positions)
    usable = (places[None, :] < kv_len[:, None])[None, :, None, None, :]
    scores = jnp.where(usable, scores, NEG)
    peak_local = jnp.max(scores, axis=-1)
    weights = jnp.where(usable, jnp.exp(scores - peak_local[..., None]), 0.0)
    mass_local = jnp.sum(weights, axis=-1)
    summed_local = jnp.einsum("jrkgc,rckd->jrkgd", weights, value_rows, precision=HIGH)
    own_heads = QHEADS // seq_count

    def by_owner(part):
        shaped = part.reshape((STEPS, rows_here, seq_count, own_heads) + part.shape[4:])
        moved = jnp.moveaxis(shaped, 2, 0)
        return moved.reshape(seq_count, -1)

    chunk_heads = local_heads // seq_count
    tail_x_parts = (
        tail_rows[0].reshape(edge, seq_count, chunk_heads * HDIM).transpose(1, 0, 2).reshape(seq_count, -1)
    )
    tail_bc = jnp.concatenate([tail_rows[1], tail_rows[2]], axis=0).reshape(seq_count, -1)
    pieces = [
        local_state.reshape(seq_count, -1),
        section_decay.reshape(seq_count, chunk_heads),
        tail_x_parts,
        tail_bc,
    ]
    peak_in, mass_in, summed_in = exchanged(
        [by_owner(peak_local), by_owner(mass_local), by_owner(summed_local)], "seq"
    )
    states_in, decays_in, tail_x_in, tail_bc_in = exchanged(pieces, "seq")

    states_in = states_in.reshape(seq_count, chunk_heads, LANES, -1)
    decays_in = decays_in[:, :chunk_heads]
    after = jnp.arange(seq_count + 1)[:, None, None]
    source = jnp.arange(seq_count)[None, :, None]
    between = jnp.arange(seq_count)[None, None, :]
    spans = ((source < between) & (between < after)).astype(jnp.float32)
    exponents = jnp.sum(spans[None] * decays_in.T[:, None, None, :], axis=-1)
    carry_weights = jnp.where((source < after)[None, :, :, 0], jnp.exp(exponents), 0.0)
    carried_all = jnp.einsum("has,shrc->ahrc", carry_weights, states_in, precision=HIGH)
    entering = carried_all[:seq_count].reshape(seq_count, -1, LANES)
    carry = carried_all[seq_count]
    returned = lax.all_to_all(entering, "seq", 0, 0, tiled=False)
    incoming = returned.reshape(local_heads, HDIM, STATE)

    state_size = chunk_heads * HDIM * STATE
    tail_size = tail_x_parts.shape[1]
    bc_size = tail_bc_in.shape[1]

    def whole_rows(value):
        return jnp.pad(value, (0, -value.shape[0] % LANES)).reshape(-1, LANES)

    handoff = jnp.concatenate(
        [
            whole_rows(carry.reshape(-1)),
            whole_rows(tail_x_in[seq_count - 1]),
            whole_rows(tail_bc_in[seq_count - 1]),
        ],
        axis=0,
    )
    swap = [
        (a * grp_count + b, b * grp_count + a) for a in range(seq_count) for b in range(grp_count)
    ]
    swapped = lax.ppermute(handoff, ("seq", "grp"), swap)
    copies = jnp.broadcast_to(swapped[None], (grp_count,) + swapped.shape)
    gathered = lax.all_to_all(copies, "grp", 0, 0, tiled=False)
    state_rows = -(-state_size // LANES)
    tail_rows_count = -(-tail_size // LANES)
    state_heads = HEADS // seq_count
    prefix_state = (
        gathered[:, :state_rows].reshape(grp_count, -1)[:, :state_size].reshape(state_heads, HDIM, STATE)
    )
    prefix_tail = (
        gathered[:, state_rows : state_rows + tail_rows_count]
        .reshape(grp_count, -1)[:, :tail_size]
        .reshape(grp_count, edge, chunk_heads * HDIM)
        .transpose(1, 0, 2)
        .reshape(edge, state_heads * HDIM)
    )
    dgroup_width = tail_rows[1].shape[1]
    tail_bc_all = (
        gathered[:, state_rows + tail_rows_count :]
        .reshape(grp_count, -1)[:, :bc_size]
        .reshape(2 * edge, dgroup_width)
    )
    tail_b = tail_bc_all[:edge]
    tail_c = tail_bc_all[edge:]

    incoming_groups = incoming.reshape(group_count, heads_each, HDIM, STATE)
    from_before = jnp.einsum("gsn,gkpn->gskp", readout, incoming_groups, precision=HIGH)
    decay_factor = jnp.exp(cumulative).reshape(group_count, heads_each, section).transpose(0, 2, 1)
    combined = intra_part + decay_factor[..., None] * from_before
    combined = (
        combined.transpose(1, 0, 2, 3).reshape(section, local_heads, HDIM)
        + gains[None, :, None] * head_inputs
    )
    pre_y = combined.reshape(section, local_heads * HDIM).astype(jnp.bfloat16)

    dec_begin = seq_index * state_heads
    dgroup_begin, dgroup_count, dheads_each = group_layout(dec_begin, state_heads)
    kernel_dx = lax.dynamic_slice_in_dim(conv_taps, dec_begin * HDIM, state_heads * HDIM, 1)
    kernel_db = lax.dynamic_slice_in_dim(
        conv_taps, x_offset + dgroup_begin * STATE, dgroup_count * STATE, 1
    )
    kernel_dc = lax.dynamic_slice_in_dim(
        conv_taps, c_offset + dgroup_begin * STATE, dgroup_count * STATE, 1
    )
    step_x = decode_conv(prefix_tail, dec_x.astype(jnp.float32), kernel_dx)
    step_b = decode_conv(
        tail_b,
        lax.dynamic_slice_in_dim(dec_b, dgroup_begin * STATE, dgroup_count * STATE, 2).astype(
            jnp.float32
        ),
        kernel_db,
    )
    step_c = decode_conv(
        tail_c,
        lax.dynamic_slice_in_dim(dec_c, dgroup_begin * STATE, dgroup_count * STATE, 2).astype(
            jnp.float32
        ),
        kernel_dc,
    )
    heads_x = step_x.reshape(STEPS, rows_here, state_heads, HDIM)
    heads_b = jnp.repeat(step_b.reshape(STEPS, rows_here, dgroup_count, STATE), dheads_each, axis=2)
    heads_c = jnp.repeat(step_c.reshape(STEPS, rows_here, dgroup_count, STATE), dheads_each, axis=2)
    dec_rates = lax.dynamic_slice_in_dim(decay_rate, dec_begin, state_heads, 0)
    dec_gains = lax.dynamic_slice_in_dim(skip_gain, dec_begin, state_heads, 0)
    mamba_out = decode_mamba(prefix_state, heads_x, heads_b, heads_c, dec_dt, dec_rates, dec_gains)
    dec_y = mamba_out.reshape(STEPS, rows_here, state_heads * HDIM).astype(jnp.bfloat16)

    head_start = seq_index * own_heads
    new_keys = new_kv[0].reshape(STEPS, rows_here, KVHEADS, ADIM)
    new_values = new_kv[1].reshape(STEPS, rows_here, KVHEADS, ADIM).astype(jnp.float32)
    new_scores = (
        jnp.einsum("jrkgd,irkd->jrkgi", queries, new_keys, preferred_element_type=jnp.float32)
        * score_scale
    )
    allowed = (jnp.arange(STEPS)[None, :] <= jnp.arange(STEPS)[:, None])[:, None, None, None, :]
    new_scores = jnp.where(allowed, new_scores, NEG)
    new_scores = lax.dynamic_slice_in_dim(
        new_scores.reshape(STEPS, rows_here, QHEADS, STEPS), head_start, own_heads, 2
    )
    allowed_heads = (jnp.arange(STEPS)[None, :] <= jnp.arange(STEPS)[:, None])[:, None, None, :]
    head_kv = (head_start + jnp.arange(own_heads)) // group_size
    pick = (head_kv[:, None] == jnp.arange(KVHEADS)[None, :]).astype(jnp.float32)
    own_values = jnp.einsum("hk,irkd->irhd", pick, new_values, precision=HIGH)
    peak_in = peak_in.reshape(seq_count, STEPS, rows_here, own_heads)
    mass_in = mass_in.reshape(seq_count, STEPS, rows_here, own_heads)
    summed_in = summed_in.reshape(seq_count, STEPS, rows_here, own_heads, ADIM)
    peak_cache = jnp.max(peak_in, axis=0)
    part_scale = jnp.exp(peak_in - peak_cache[None])
    mass_cache = jnp.sum(mass_in * part_scale, axis=0)
    summed_cache = jnp.sum(summed_in * part_scale[..., None], axis=0)
    peak_total = jnp.maximum(peak_cache, jnp.max(new_scores, axis=-1))
    cache_scale = jnp.exp(peak_cache - peak_total)
    new_weights = jnp.where(allowed_heads, jnp.exp(new_scores - peak_total[..., None]), 0.0)
    mass_total = mass_cache * cache_scale + jnp.sum(new_weights, axis=-1)
    summed_total = summed_cache * cache_scale[..., None] + jnp.einsum(
        "jrhi,irhd->jrhd", new_weights, own_values, precision=HIGH
    )
    attn_out = (
        (summed_total / mass_total[..., None])
        .reshape(STEPS, rows_here, own_heads * ADIM)
        .astype(jnp.bfloat16)
    )
    return (pre_y, dec_y, attn_out)


def solution(mesh):
    in_specs = (
        P("seq", "grp"),
        P("seq", None),
        P("seq", None),
        P("grp", "seq"),
        P(),
        P(),
        P(),
        P(None, "grp", "seq"),
        P(None, "grp", None),
        P(None, "grp", None),
        P(None, "grp", "seq"),
        P(None, "grp", None),
        P(None, None, "grp", None),
        P(None, "grp", "seq", None),
        P("grp"),
    )
    out_specs = (P("seq", "grp"), P(None, "grp", "seq"), P(None, "grp", "seq"))

    return jax.shard_map(on_device, mesh=mesh, in_specs=in_specs, out_specs=out_specs, check_vma=False)
```

```python
import jax
import jax.numpy as jnp
from jax import lax
from jax.sharding import PartitionSpec as P

HEADS = 256
HDIM = 64
STATE = 256
GROUPS = 8
TAPS = 4
QHEADS = 64
KVHEADS = 8
ADIM = 128
SPAN = 256
STEPS = 2


HIGH = lax.Precision.HIGHEST
NEG = -1e30


LANES = 128


def exchanged(pieces, axis):
    count = pieces[0].shape[0]
    sizes = [piece.shape[1] for piece in pieces]
    rows = [-(-size // LANES) for size in sizes]
    packed = jnp.concatenate(
        [
            jnp.pad(piece, ((0, 0), (0, row * LANES - size))).reshape(count, row, LANES)
            for piece, size, row in zip(pieces, sizes, rows)
        ],
        axis=1,
    )
    arrived = lax.all_to_all(packed, axis, 0, 0, tiled=False)
    results = []
    begin = 0
    for size, row in zip(sizes, rows):
        results.append(arrived[:, begin : begin + row].reshape(count, row * LANES)[:, :size])
        begin += row
    return results


def passed_along(value, axis, steps):
    count = lax.axis_size(axis)
    first, last = (max(0, -steps), min(count, count - steps))
    return lax.ppermute(value, axis, [(source, source + steps) for source in range(first, last)])


def causal_conv(leading, source, kernel):
    row_total = source.shape[0]
    padded = jnp.concatenate([leading, source], axis=0)
    accumulated = jnp.zeros_like(source)
    for position in range(TAPS):
        accumulated = accumulated + kernel[position] * padded[position : position + row_total]
    return jax.nn.silu(accumulated)


def decode_conv(leading, fresh, kernel):
    results = []
    for current in range(fresh.shape[0]):
        accumulated = jnp.zeros(fresh.shape[1:], jnp.float32)
        for position in range(TAPS):
            place = current + position
            if place < TAPS - 1:
                term = leading[place][None, :]
            else:
                term = fresh[place - (TAPS - 1)]
            accumulated = accumulated + kernel[position] * term
        results.append(jax.nn.silu(accumulated))
    return jnp.stack(results)


def span_pass(ssm_state, block):
    inputs, entries, readout, log_decay = block
    cumulative = jnp.cumsum(log_decay, axis=1)
    block_size = log_decay.shape[1]
    causal = jnp.arange(block_size)[:, None] >= jnp.arange(block_size)[None, :]
    spreads = cumulative[:, :, None] - cumulative[:, None, :]
    weights = jnp.where(causal[None], jnp.exp(jnp.where(causal[None], spreads, 0.0)), 0.0)
    intersection = jnp.dot(readout, entries.T, precision=HIGH)
    intra_span = jnp.einsum("kts,skp->tkp", weights * intersection[None], inputs, precision=HIGH)
    carried = jnp.exp(cumulative).T[:, :, None] * jnp.einsum(
        "tn,kpn->tkp", readout, ssm_state, precision=HIGH
    )
    remaining = jnp.exp(cumulative[:, -1:] - cumulative)
    updates = jnp.einsum("skp,sn->kpn", inputs * remaining.T[:, :, None], entries, precision=HIGH)
    renewed = jnp.exp(cumulative[:, -1])[:, None, None] * ssm_state + updates
    return (renewed, intra_span + carried)


def decode_mamba(ssm_state, heads_x, group_b, group_c, step_dt, rates, gains):
    steps, rows, group_count, heads_each, width = heads_x.shape
    shaped = lambda value: value.reshape(steps, rows, group_count, heads_each)
    decays = shaped(jnp.exp(-step_dt * rates))
    step_dt = shaped(step_dt)
    gains = gains.reshape(group_count, heads_each)
    grouped_state = ssm_state.reshape(group_count, heads_each, width, -1)
    from_prefix = jnp.einsum("jrgn,gepn->jrgep", group_c, grouped_state, precision=HIGH)
    results = []
    for current in range(steps):
        factor = jnp.ones(decays.shape[1:], jnp.float32)
        accumulated = gains[None, :, :, None] * heads_x[current]
        for earlier in range(current, -1, -1):
            intersection = jnp.sum(group_c[current] * group_b[earlier], axis=-1)
            accumulated = (
                accumulated
                + (factor * step_dt[earlier] * intersection[..., None])[..., None]
                * heads_x[earlier]
            )
            factor = factor * decays[earlier]
        accumulated = accumulated + factor[..., None] * from_prefix[current]
        results.append(accumulated)
    return jnp.stack(results)


def run_spans(inputs, entries, readout, log_decay, ssm_state):
    row_total, _, _ = inputs.shape
    block_total = row_total // SPAN
    results = []
    for block in range(block_total):
        rows = slice(block * SPAN, (block + 1) * SPAN)
        ssm_state, result = span_pass(
            ssm_state, (inputs[rows], entries[rows], readout[rows], log_decay[:, rows])
        )
        results.append(result)
    return (jnp.concatenate(results, axis=0), ssm_state)


def group_layout(head_begin, head_count):
    per_group = HEADS // GROUPS
    group_count = max(1, head_count // per_group)
    return (head_begin // per_group, group_count, head_count // group_count)


def on_device(
    pre_x,
    pre_b,
    pre_c,
    pre_dt,
    decay_rate,
    skip_gain,
    conv_taps,
    dec_x,
    dec_b,
    dec_c,
    dec_dt,
    dec_query,
    new_kv,
    cache_kv,
    kv_len,
):
    seq_count = lax.axis_size("seq")
    grp_count = lax.axis_size("grp")
    seq_index = lax.axis_index("seq")
    grp_index = lax.axis_index("grp")
    section = pre_x.shape[0]
    local_heads = pre_x.shape[1] // HDIM
    edge = TAPS - 1
    x_offset = HEADS * HDIM
    c_offset = HEADS * HDIM + GROUPS * STATE
    head_begin = grp_index * local_heads
    group_begin, group_count, heads_each = group_layout(head_begin, local_heads)
    source_x = pre_x.astype(jnp.float32)
    group_b = lax.dynamic_slice_in_dim(pre_b, group_begin * STATE, group_count * STATE, 1).astype(
        jnp.float32
    )
    group_c = lax.dynamic_slice_in_dim(pre_c, group_begin * STATE, group_count * STATE, 1).astype(
        jnp.float32
    )
    tail_rows = (source_x[section - edge :], group_b[section - edge :], group_c[section - edge :])
    leading = passed_along(tail_rows, "seq", 1)
    kernel_x = lax.dynamic_slice_in_dim(conv_taps, head_begin * HDIM, local_heads * HDIM, 1)
    kernel_b = lax.dynamic_slice_in_dim(
        conv_taps, x_offset + group_begin * STATE, group_count * STATE, 1
    )
    kernel_c = lax.dynamic_slice_in_dim(
        conv_taps, c_offset + group_begin * STATE, group_count * STATE, 1
    )
    conv_x = causal_conv(leading[0], source_x, kernel_x)
    conv_b = causal_conv(leading[1], group_b, kernel_b)
    conv_c = causal_conv(leading[2], group_c, kernel_c)
    rates = lax.dynamic_slice_in_dim(decay_rate, head_begin, local_heads, 0)
    gains = lax.dynamic_slice_in_dim(skip_gain, head_begin, local_heads, 0)
    log_decay = -pre_dt * rates[:, None]
    head_inputs = conv_x.reshape(section, local_heads, HDIM)
    scaled = head_inputs * pre_dt.T[:, :, None]
    grouped = scaled.reshape(section, group_count, heads_each, HDIM).transpose(1, 0, 2, 3)
    entries = conv_b.reshape(section, group_count, STATE).transpose(1, 0, 2)
    readout = conv_c.reshape(section, group_count, STATE).transpose(1, 0, 2)
    decay_groups = log_decay.reshape(group_count, heads_each, section)
    blank = jnp.zeros((group_count, heads_each, HDIM, STATE), jnp.float32)
    intra_part, closing_local = jax.vmap(run_spans)(grouped, entries, readout, decay_groups, blank)
    local_state = closing_local.reshape(local_heads, HDIM, STATE)
    cumulative = jnp.cumsum(log_decay, axis=1)
    section_decay = cumulative[:, -1]

    rows_here = dec_x.shape[1]
    group_size = QHEADS // KVHEADS
    score_scale = ADIM ** (-0.5)
    positions = cache_kv.shape[2]
    queries = dec_query.reshape(STEPS, rows_here, KVHEADS, group_size, ADIM)
    key_rows = cache_kv[0].reshape(rows_here, positions, KVHEADS, ADIM)
    value_rows = cache_kv[1].reshape(rows_here, positions, KVHEADS, ADIM).astype(jnp.float32)
    scores = (
        jnp.einsum("jrkgd,rckd->jrkgc", queries, key_rows, preferred_element_type=jnp.float32)
        * score_scale
    )
    places = seq_index * positions + jnp.arange(positions)
    usable = (places[None, :] < kv_len[:, None])[None, :, None, None, :]
    scores = jnp.where(usable, scores, NEG)
    peak_local = jnp.max(scores, axis=-1)
    weights = jnp.where(usable, jnp.exp(scores - peak_local[..., None]), 0.0)
    mass_local = jnp.sum(weights, axis=-1)
    summed_local = jnp.einsum("jrkgc,rckd->jrkgd", weights, value_rows, precision=HIGH)
    own_heads = QHEADS // seq_count

    def by_owner(part):
        shaped = part.reshape((STEPS, rows_here, seq_count, own_heads) + part.shape[4:])
        moved = jnp.moveaxis(shaped, 2, 0)
        return moved.reshape(seq_count, -1)

    chunk_heads = local_heads // seq_count
    tail_x_parts = (
        tail_rows[0].reshape(edge, seq_count, chunk_heads * HDIM).transpose(1, 0, 2).reshape(seq_count, -1)
    )
    tail_bc = jnp.concatenate([tail_rows[1], tail_rows[2]], axis=0).reshape(seq_count, -1)
    pieces = [
        local_state.reshape(seq_count, -1),
        section_decay.reshape(seq_count, chunk_heads),
        tail_x_parts,
        tail_bc,
    ]
    peak_in, mass_in, summed_in = exchanged(
        [by_owner(peak_local), by_owner(mass_local), by_owner(summed_local)], "seq"
    )
    states_in, decays_in, tail_x_in, tail_bc_in = exchanged(pieces, "seq")

    states_in = states_in.reshape(seq_count, chunk_heads, LANES, -1)
    decays_in = decays_in[:, :chunk_heads]
    after = jnp.arange(seq_count + 1)[:, None, None]
    source = jnp.arange(seq_count)[None, :, None]
    between = jnp.arange(seq_count)[None, None, :]
    spans = ((source < between) & (between < after)).astype(jnp.float32)
    exponents = jnp.sum(spans[None] * decays_in.T[:, None, None, :], axis=-1)
    carry_weights = jnp.where((source < after)[None, :, :, 0], jnp.exp(exponents), 0.0)
    carried_all = jnp.einsum("has,shrc->ahrc", carry_weights, states_in, precision=HIGH)
    entering = carried_all[:seq_count].reshape(seq_count, -1, LANES)
    carry = carried_all[seq_count]
    returned = lax.all_to_all(entering, "seq", 0, 0, tiled=False)
    incoming = returned.reshape(local_heads, HDIM, STATE)

    state_size = chunk_heads * HDIM * STATE
    tail_size = tail_x_parts.shape[1]
    handoff = jnp.concatenate(
        [carry.reshape(-1), tail_x_in[seq_count - 1], tail_bc_in[seq_count - 1]], axis=0
    )
    handoff = jnp.pad(handoff, (0, -handoff.shape[0] % LANES)).reshape(-1, LANES)
    swap = [
        (a * grp_count + b, b * grp_count + a) for a in range(seq_count) for b in range(grp_count)
    ]
    swapped = lax.ppermute(handoff, ("seq", "grp"), swap)
    copies = jnp.broadcast_to(swapped[None], (grp_count,) + swapped.shape)
    gathered = lax.all_to_all(copies, "grp", 0, 0, tiled=False).reshape(grp_count, -1)
    state_heads = HEADS // seq_count
    prefix_state = gathered[:, :state_size].reshape(state_heads, HDIM, STATE)
    prefix_tail = (
        gathered[:, state_size : state_size + tail_size]
        .reshape(grp_count, edge, chunk_heads * HDIM)
        .transpose(1, 0, 2)
        .reshape(edge, state_heads * HDIM)
    )
    dgroup_width = tail_rows[1].shape[1]
    bc_size = 2 * edge * dgroup_width // grp_count
    tail_bc_all = gathered[:, state_size + tail_size : state_size + tail_size + bc_size].reshape(
        2 * edge, dgroup_width
    )
    tail_b = tail_bc_all[:edge]
    tail_c = tail_bc_all[edge:]

    incoming_groups = incoming.reshape(group_count, heads_each, HDIM, STATE)
    from_before = jnp.einsum("gsn,gkpn->gskp", readout, incoming_groups, precision=HIGH)
    decay_factor = jnp.exp(cumulative).reshape(group_count, heads_each, section).transpose(0, 2, 1)
    combined = intra_part + decay_factor[..., None] * from_before
    combined = (
        combined.transpose(1, 0, 2, 3).reshape(section, local_heads, HDIM)
        + gains[None, :, None] * head_inputs
    )
    pre_y = combined.reshape(section, local_heads * HDIM).astype(jnp.bfloat16)

    dec_begin = seq_index * state_heads
    dgroup_begin, dgroup_count, dheads_each = group_layout(dec_begin, state_heads)
    kernel_dx = lax.dynamic_slice_in_dim(conv_taps, dec_begin * HDIM, state_heads * HDIM, 1)
    kernel_db = lax.dynamic_slice_in_dim(
        conv_taps, x_offset + dgroup_begin * STATE, dgroup_count * STATE, 1
    )
    kernel_dc = lax.dynamic_slice_in_dim(
        conv_taps, c_offset + dgroup_begin * STATE, dgroup_count * STATE, 1
    )
    step_x = decode_conv(prefix_tail, dec_x.astype(jnp.float32), kernel_dx)
    step_b = decode_conv(
        tail_b,
        lax.dynamic_slice_in_dim(dec_b, dgroup_begin * STATE, dgroup_count * STATE, 2).astype(
            jnp.float32
        ),
        kernel_db,
    )
    step_c = decode_conv(
        tail_c,
        lax.dynamic_slice_in_dim(dec_c, dgroup_begin * STATE, dgroup_count * STATE, 2).astype(
            jnp.float32
        ),
        kernel_dc,
    )
    heads_x = step_x.reshape(STEPS, rows_here, dgroup_count, dheads_each, HDIM)
    group_b = step_b.reshape(STEPS, rows_here, dgroup_count, STATE)
    group_c = step_c.reshape(STEPS, rows_here, dgroup_count, STATE)
    dec_rates = lax.dynamic_slice_in_dim(decay_rate, dec_begin, state_heads, 0)
    dec_gains = lax.dynamic_slice_in_dim(skip_gain, dec_begin, state_heads, 0)
    mamba_out = decode_mamba(prefix_state, heads_x, group_b, group_c, dec_dt, dec_rates, dec_gains)
    dec_y = mamba_out.reshape(STEPS, rows_here, state_heads * HDIM).astype(jnp.bfloat16)

    head_start = seq_index * own_heads
    new_keys = new_kv[0].reshape(STEPS, rows_here, KVHEADS, ADIM)
    new_values = new_kv[1].reshape(STEPS, rows_here, KVHEADS, ADIM).astype(jnp.float32)
    new_scores = (
        jnp.einsum("jrkgd,irkd->jrkgi", queries, new_keys, preferred_element_type=jnp.float32)
        * score_scale
    )
    allowed = (jnp.arange(STEPS)[None, :] <= jnp.arange(STEPS)[:, None])[:, None, None, None, :]
    new_scores = jnp.where(allowed, new_scores, NEG)
    new_scores = lax.dynamic_slice_in_dim(
        new_scores.reshape(STEPS, rows_here, QHEADS, STEPS), head_start, own_heads, 2
    )
    allowed_heads = (jnp.arange(STEPS)[None, :] <= jnp.arange(STEPS)[:, None])[:, None, None, :]
    head_kv = (head_start + jnp.arange(own_heads)) // group_size
    pick = (head_kv[:, None] == jnp.arange(KVHEADS)[None, :]).astype(jnp.float32)
    own_values = jnp.einsum("hk,irkd->irhd", pick, new_values, precision=HIGH)
    peak_in = peak_in.reshape(seq_count, STEPS, rows_here, own_heads)
    mass_in = mass_in.reshape(seq_count, STEPS, rows_here, own_heads)
    summed_in = summed_in.reshape(seq_count, STEPS, rows_here, own_heads, ADIM)
    peak_cache = jnp.max(peak_in, axis=0)
    part_scale = jnp.exp(peak_in - peak_cache[None])
    mass_cache = jnp.sum(mass_in * part_scale, axis=0)
    summed_cache = jnp.sum(summed_in * part_scale[..., None], axis=0)
    peak_total = jnp.maximum(peak_cache, jnp.max(new_scores, axis=-1))
    cache_scale = jnp.exp(peak_cache - peak_total)
    new_weights = jnp.where(allowed_heads, jnp.exp(new_scores - peak_total[..., None]), 0.0)
    mass_total = mass_cache * cache_scale + jnp.sum(new_weights, axis=-1)
    summed_total = summed_cache * cache_scale[..., None] + jnp.einsum(
        "jrhi,irhd->jrhd", new_weights, own_values, precision=HIGH
    )
    attn_out = (
        (summed_total / mass_total[..., None])
        .reshape(STEPS, rows_here, own_heads * ADIM)
        .astype(jnp.bfloat16)
    )
    return (pre_y, dec_y, attn_out)


def solution(mesh):
    in_specs = (
        P("seq", "grp"),
        P("seq", None),
        P("seq", None),
        P("grp", "seq"),
        P(),
        P(),
        P(),
        P(None, "grp", "seq"),
        P(None, "grp", None),
        P(None, "grp", None),
        P(None, "grp", "seq"),
        P(None, "grp", None),
        P(None, None, "grp", None),
        P(None, "grp", "seq", None),
        P("grp"),
    )
    out_specs = (P("seq", "grp"), P(None, "grp", "seq"), P(None, "grp", "seq"))

    return jax.shard_map(on_device, mesh=mesh, in_specs=in_specs, out_specs=out_specs, check_vma=False)
```
